256 devices in a mesh: blk: 8 (over x, y_lo), grp: 32 (over y_hi, z, core).
Axes of the slice: x: 4, y: 4 (y_hi: 2, y_lo: 2; y = y_hi * 2 + y_lo), z: 8, core: 2. Of those that a mesh axis runs over, the one named last changes fastest.
Arguments:
- centres: float32 [3, 262144], P(None, ('blk', 'grp')), may hold values from -32 to 32, as said below
- coeffs: float32 [3, 262144], P(None, ('blk', 'grp')), may hold values from -2 to 5.5
- residual: float32 [3, 262144], P(None, ('blk', 'grp')), may hold values from -18 to 18
- direction_prev: float32 [3, 262144], P(None, ('blk', 'grp')), may hold values from -6 to 6
- smoothing: float32 [262144], P(('blk', 'grp')), may hold values from 0.5 to 5
- norm_prev: float32 [3], replicated, may hold values from 262144 to 1048576
- support_radius: int32 [1], replicated, may hold values from 900 to 960
- volume_nodes: float32 [3, 262144], P(None, ('blk', 'grp')), may hold values from -34 to 34
- block_lists: int32 [256, 4], P(('blk', 'grp')), may hold values from 0 to 31, as said below
Outputs:
- coeffs_next: float32 [3, 262144], P(None, ('blk', 'grp'))
- residual_next: float32 [3, 262144], P(None, ('blk', 'grp'))
- direction: float32 [3, 262144], P(None, ('blk', 'grp'))
- norm_next: float32 [3], replicated
- displacement: float32 [3, 262144], P(None, ('blk', 'grp'))
The draws below stay inside these ranges and needn't reach their ends.
Inputs may be any that keep to these rules, and one draw needn't show every extreme that they name: `centres`: every centre of block k has its distance from the z axis within [g, g + 1) with g = k mod 32, and lies at height -0.01 times the square of that distance. `block_lists`: each row names 4 different bands.
All inputs are finite; a program needn't handle non-finite values.
Results may differ from the reference program's by a relative error of at most 0.0003.
Values sent between devices are 32-bit elements; how exact they have to be, the bound alone decides.
No kernel may reach another device: no remote copies, remote signals or barrier semaphores. Data moves between devices by JAX's collectives and lax.ppermute only.
A program may use at most 64 MiB of HBM per device.

```python
import math
import jax
import jax.numpy as jnp
from jax import lax

C_DEV = 1024
V_DEV = 1024
LIST = 4
NC = 262144
N_BLK = 8
N_GRP = 32


CURVE = 0.01


def band_lists(key):
    inner = jax.random.fold_in(key, 17)
    total = N_BLK * N_GRP
    scores = jax.random.randint(inner, (total, N_GRP), 0, 1 << 20) * N_GRP + jnp.arange(N_GRP, dtype=jnp.int32)[None, :]
    order = jnp.argsort(scores, axis=1)
    return order[:, :LIST].astype(jnp.int32)


def draw_block_lists(key, part):
    return band_lists(key)


def draw_volume_nodes(key, part):
    lists = band_lists(key)
    total = N_BLK * N_GRP
    inner = jax.random.fold_in(key, 29)
    first, second, third = jax.random.split(inner, 3)
    slot = jnp.arange(V_DEV) % LIST
    bands = lists[:, slot].astype(jnp.float32)
    sector = (jnp.arange(total) // N_GRP).astype(jnp.float32)[:, None]
    turn = jax.random.uniform(first, (total, V_DEV), jnp.float32)
    angle = 2.0 * math.pi * (sector + turn) / N_BLK
    offset = jax.random.uniform(second, (total, V_DEV), jnp.float32, -0.5, 1.5)
    distance = jnp.maximum(bands + offset, 0.0)
    lift = jax.random.uniform(third, (total, V_DEV), jnp.float32, 0.8, 0.9)
    stacked = jnp.stack([distance * jnp.cos(angle), distance * jnp.sin(angle), lift - CURVE * distance * distance])
    return stacked.reshape(3, total * V_DEV)


def draw_centres(key, part):
    total = N_BLK * N_GRP
    inner = jax.random.fold_in(key, 41)
    first, second = jax.random.split(inner, 2)
    sector = (jnp.arange(total) // N_GRP).astype(jnp.float32)[:, None]
    band = (jnp.arange(total) % N_GRP).astype(jnp.float32)[:, None]
    turn = jax.random.uniform(first, (total, C_DEV), jnp.float32)
    radial = jax.random.uniform(second, (total, C_DEV), jnp.float32)
    angle = 2.0 * math.pi * (sector + turn) / N_BLK
    distance = band + radial
    stacked = jnp.stack([distance * jnp.cos(angle), distance * jnp.sin(angle), -CURVE * distance * distance])
    return stacked.reshape(3, total * C_DEV)


def draw_coeffs(key, part):
    total = N_BLK * N_GRP
    inner = jax.random.fold_in(key, 67)
    values = 1.5 + 0.8 * jnp.clip(jax.random.normal(inner, (3, total * C_DEV), jnp.float32), -4.0, 4.0)
    return values


def draw_residual(key, part):
    total = N_BLK * N_GRP
    inner = jax.random.fold_in(key, 53)
    rising = jnp.exp(math.log(3.0) * jnp.arange(total, dtype=jnp.float32) / (total - 1))
    base = jnp.clip(jax.random.normal(inner, (3, total, C_DEV), jnp.float32), -6.0, 6.0)
    return (base * rising[None, :, None]).reshape(3, total * C_DEV)


def block_levels(rng, shape, pieces, smallest, high):
    loudness = 1.0
    for axis_at, parts in pieces:
        draws = jax.random.uniform(jax.random.fold_in(jax.random.fold_in(rng, 6), axis_at), (parts,), jnp.float32, smallest / len(pieces), high / len(pieces))
        loudness = loudness * jnp.repeat(jnp.exp(draws), shape[axis_at] // parts).reshape((-1,) + (1,) * (len(shape) - 1 - axis_at))
    return loudness


def noise(stream_key, shape, scale, most, cuts=(), kind=jnp.bfloat16):
    factor_of = block_levels(stream_key, shape, cuts, -0.22, 0.18) if cuts else 1.0
    array = jax.random.normal(stream_key, shape, jnp.float32) * scale * factor_of
    return jnp.minimum(jnp.maximum(array, -most), most).astype(kind)


def setup_inputs(seed: int = 0) -> dict:
    keys = jax.random.split(jax.random.key(seed), 10)
    centres = draw_centres(jax.random.fold_in(keys[9], 71), 0)
    coeffs = draw_coeffs(jax.random.fold_in(keys[9], 71), 0)
    residual = draw_residual(jax.random.fold_in(keys[9], 71), 0)
    direction_prev = noise(keys[3], (3, NC), 1.0, 6.0, ((1, 256),), jnp.float32)
    smoothing = jnp.clip(jnp.exp(math.log(5.0) - 2.3025851 * jax.random.uniform(keys[4], (NC,), jnp.float32) ** block_levels(keys[4], (NC,), ((0, 256),), -0.2, 0.2)), 0.5, 5.0)
    norm_prev = jnp.clip(jnp.exp(jax.random.uniform(keys[5], (3,), jnp.float32, math.log(262144.0), math.log(1048576))), 262144.0, 1048576)
    support_radius = jax.random.randint(keys[6], (1,), 900, 961).astype(jnp.int32)
    volume_nodes = draw_volume_nodes(jax.random.fold_in(keys[9], 71), 0)
    block_lists = draw_block_lists(jax.random.fold_in(keys[9], 71), 0)
    return {"centres": centres, "coeffs": coeffs, "residual": residual, "direction_prev": direction_prev, "smoothing": smoothing, "norm_prev": norm_prev, "support_radius": support_radius, "volume_nodes": volume_nodes, "block_lists": block_lists}


RADIUS_UNIT = 0.001

def wendland(sources, targets, radius):
    apart_first = sources[0][:, None] - targets[0][None, :]
    apart_second = sources[1][:, None] - targets[1][None, :]
    apart_third = sources[2][:, None] - targets[2][None, :]
    distance = jnp.sqrt(apart_first * apart_first + apart_second * apart_second + apart_third * apart_third)
    scaled = distance / radius
    remain = jnp.maximum(1.0 - scaled, 0.0)
    square = remain * remain
    return square * square * (4.0 * scaled + 1.0)

def kernel_product(centres, direction, radius):
    total = N_BLK * N_GRP
    count = centres.shape[1] // total
    zero = jnp.zeros((), jnp.int32)
    places = centres.reshape(3, N_BLK, N_GRP, count)
    values = direction.reshape(3, N_BLK, N_GRP, count)
    padding = jnp.zeros((3, N_BLK, 1, count), jnp.float32)
    places_pad = jnp.concatenate([padding, places, padding], axis=2)
    values_pad = jnp.concatenate([padding, values, padding], axis=2)

    def one_block(index):
        sector = index // N_GRP
        band = index % N_GRP
        targets = lax.dynamic_slice(places, (zero, sector, band, zero), (3, 1, 1, count)).reshape(3, count)
        near_places = lax.dynamic_slice(places_pad, (zero, zero, band, zero), (3, N_BLK, 3, count)).reshape(3, N_BLK * 3 * count)
        near_values = lax.dynamic_slice(values_pad, (zero, zero, band, zero), (3, N_BLK, 3, count)).reshape(3, N_BLK * 3 * count)
        weights = wendland(near_places, targets, radius)
        return jnp.dot(near_values, weights, preferred_element_type=jnp.float32, precision=lax.Precision.HIGHEST)
    result = lax.map(one_block, jnp.arange(total, dtype=jnp.int32))
    return result.transpose(1, 0, 2).reshape(3, total * count)

def evaluate(centres, coeffs_next, volume_nodes, block_lists, radius):
    total = N_BLK * N_GRP
    count = centres.shape[1] // total
    per_block = volume_nodes.shape[1] // total
    zero = jnp.zeros((), jnp.int32)
    places = centres.reshape(3, N_BLK, N_GRP, count)
    values = coeffs_next.reshape(3, N_BLK, N_GRP, count)
    nodes = volume_nodes.reshape(3, total, per_block)

    def one_block(index):
        sector = index // N_GRP
        targets = lax.dynamic_slice(nodes, (zero, index, zero), (3, 1, per_block)).reshape(3, per_block)
        listed = block_lists[index]

        def one_entry(carry, band):
            band = band.astype(jnp.int32)
            sources = lax.dynamic_slice(places, (zero, sector, band, zero), (3, 1, 1, count)).reshape(3, count)
            weights_in = lax.dynamic_slice(values, (zero, sector, band, zero), (3, 1, 1, count)).reshape(3, count)
            weights = wendland(sources, targets, radius)
            return (carry + jnp.dot(weights_in, weights, preferred_element_type=jnp.float32, precision=lax.Precision.HIGHEST), None)
        result, _ = lax.scan(one_entry, jnp.zeros((3, per_block), jnp.float32), listed)
        return result
    result = lax.map(one_block, jnp.arange(total, dtype=jnp.int32))
    return result.transpose(1, 0, 2).reshape(3, total * per_block)

def reference(centres, coeffs, residual, direction_prev, smoothing, norm_prev, support_radius, volume_nodes, block_lists):
    radius = support_radius[0].astype(jnp.float32) * RADIUS_UNIT
    scaling = 1.0 + smoothing
    precond = residual / scaling
    norm_now = lax.optimization_barrier(jnp.sum(residual * precond, axis=1))
    beta = norm_now / norm_prev
    direction = precond + beta[:, None] * direction_prev
    image = smoothing * direction + kernel_product(centres, direction, radius)
    curvature = lax.optimization_barrier(jnp.sum(direction * image, axis=1))
    alpha = norm_now / curvature
    coeffs_next = coeffs + alpha[:, None] * direction
    residual_next = residual - alpha[:, None] * image
    norm_next = lax.optimization_barrier(jnp.sum(residual_next * residual_next / scaling, axis=1))
    displacement = evaluate(centres, coeffs_next, volume_nodes, block_lists, radius)
    return (coeffs_next, residual_next, direction, norm_next, displacement)
```

```python
import jax
import jax.numpy as jnp
from jax import lax
from jax.sharding import PartitionSpec as P

RADIUS_UNIT = 0.001


def xor_pairs(size, mask):
    return [(i, i ^ mask) for i in range(size)]


def all_sum(value):
    for axis in ("grp", "blk"):
        size = lax.axis_size(axis)
        mask = 1
        while mask < size:
            value = value + lax.ppermute(value, axis, xor_pairs(size, mask))
            mask *= 2
    return value


def wendland(sources, targets, radius):
    apart_first = sources[0][:, None] - targets[0][None, :]
    apart_second = sources[1][:, None] - targets[1][None, :]
    apart_third = sources[2][:, None] - targets[2][None, :]
    distance = jnp.sqrt(
        apart_first * apart_first + apart_second * apart_second + apart_third * apart_third
    )
    scaled = distance / radius
    remain = jnp.maximum(1.0 - scaled, 0.0)
    square = remain * remain
    return square * square * (4.0 * scaled + 1.0)


def apply_block(total, block, targets, radius):
    weights = wendland(block[:3], targets, radius)
    return total + jnp.dot(
        block[3:], weights, preferred_element_type=jnp.float32, precision=lax.Precision.HIGHEST
    )


def apply_piece(total, piece, targets, count, radius):
    for index in range(piece.shape[1] // count):
        total = apply_block(total, piece[:, index * count:(index + 1) * count], targets, radius)
    return total


def per_device(
    centres,
    coeffs,
    residual,
    direction_prev,
    smoothing,
    norm_prev,
    support_radius,
    volume_nodes,
    block_lists,
):
    radius = support_radius[0].astype(jnp.float32) * RADIUS_UNIT
    count = centres.shape[1]
    n_grp = lax.axis_size("grp")
    n_blk = lax.axis_size("blk")
    scaling = 1.0 + smoothing
    precond = residual / scaling
    norm_now = all_sum(jnp.sum(residual * precond, axis=1))

    bundle = jnp.concatenate([centres, precond, direction_prev], axis=0)
    up = [(i, i + 1) for i in range(n_grp - 1)]
    down = [(i + 1, i) for i in range(n_grp - 1)]
    before = lax.ppermute(bundle, "grp", up)
    after = lax.ppermute(bundle, "grp", down)
    widened = jnp.concatenate([before, bundle, after], axis=1)
    arrivals = [lax.ppermute(widened, "blk", xor_pairs(n_blk, mask)) for mask in range(1, n_blk)]

    total = jnp.zeros((6, count), jnp.float32)
    total = apply_piece(total, widened, centres, count, radius)
    for piece in arrivals:
        total = apply_piece(total, piece, centres, count, radius)

    beta = norm_now / norm_prev
    direction = precond + beta[:, None] * direction_prev
    image = smoothing * direction + (total[:3] + beta[:, None] * total[3:])

    gathered = jnp.concatenate([centres, coeffs, direction], axis=0)
    masks = []
    mask = n_grp // 2
    while mask >= 1:
        gathered = jnp.concatenate(
            [gathered, lax.ppermute(gathered, "grp", xor_pairs(n_grp, mask))], axis=1
        )
        masks.append(mask)
        mask //= 2

    partial = jnp.concatenate(
        [
            jnp.sum(direction * image, axis=1),
            jnp.sum(residual * residual / scaling, axis=1),
            jnp.sum(residual * image / scaling, axis=1),
            jnp.sum(image * image / scaling, axis=1),
        ]
    )
    sums = all_sum(partial)
    curvature = sums[0:3]
    alpha = norm_now / curvature
    coeffs_next = coeffs + alpha[:, None] * direction
    residual_next = residual - alpha[:, None] * image
    norm_next = sums[3:6] - 2.0 * alpha * sums[6:9] + alpha * alpha * sums[9:12]

    me = lax.axis_index("grp")
    listed = block_lists[0]
    evaluation = jnp.zeros((6, volume_nodes.shape[1]), jnp.float32)
    for slot in range(listed.shape[0]):
        apart = jnp.bitwise_xor(listed[slot], me)
        position = jnp.zeros((), jnp.int32)
        for bit, mask in enumerate(masks):
            position = position + ((apart // mask) % 2) * (1 << bit)
        block = lax.dynamic_slice_in_dim(gathered, position * count, count, 1)
        evaluation = apply_block(evaluation, block, volume_nodes, radius)
    displacement = evaluation[:3] + alpha[:, None] * evaluation[3:]
    return (coeffs_next, residual_next, direction, norm_next, displacement)


def solution(mesh):
    placed = (
        P(None, ("blk", "grp")),
        P(None, ("blk", "grp")),
        P(None, ("blk", "grp")),
        P(None, ("blk", "grp")),
        P(("blk", "grp")),
        P(),
        P(),
        P(None, ("blk", "grp")),
        P(("blk", "grp"), None),
    )
    return jax.shard_map(
        per_device,
        mesh=mesh,
        in_specs=placed,
        out_specs=(
            P(None, ("blk", "grp")),
            P(None, ("blk", "grp")),
            P(None, ("blk", "grp")),
            P(),
            P(None, ("blk", "grp")),
        ),
        check_vma=False,
    )
```

```python
import jax
import jax.numpy as jnp
from jax import lax
from jax.sharding import PartitionSpec as P

RADIUS_UNIT = 0.001
SKIP_MARGIN = 1.001


def xor_pairs(size, mask):
    return [(i, i ^ mask) for i in range(size)]


def all_sum(value):
    for axis in ("grp", "blk"):
        size = lax.axis_size(axis)
        mask = 1
        while mask < size:
            value = value + lax.ppermute(value, axis, xor_pairs(size, mask))
            mask *= 2
    return value


def wendland(sources, targets, radius):
    apart_first = sources[0][:, None] - targets[0][None, :]
    apart_second = sources[1][:, None] - targets[1][None, :]
    apart_third = sources[2][:, None] - targets[2][None, :]
    distance = jnp.sqrt(
        apart_first * apart_first + apart_second * apart_second + apart_third * apart_third
    )
    scaled = distance / radius
    remain = jnp.maximum(1.0 - scaled, 0.0)
    square = remain * remain
    return square * square * (4.0 * scaled + 1.0)


def box(points):
    return jnp.min(points, axis=1), jnp.max(points, axis=1)


def apply_block(total, block, targets, target_box, radius):
    low, high = box(block[:3])
    gap = jnp.maximum(jnp.maximum(target_box[0] - high, low - target_box[1]), 0.0)
    far = jnp.sum(gap * gap) > (radius * SKIP_MARGIN) * (radius * SKIP_MARGIN)

    def near(total):
        weights = wendland(block[:3], targets, radius)
        return total + jnp.dot(
            block[3:], weights, preferred_element_type=jnp.float32, precision=lax.Precision.HIGHEST
        )

    return lax.cond(far, lambda total: total, near, total)


def apply_piece(total, piece, targets, target_box, count, radius):
    def one(index, total):
        block = lax.dynamic_slice_in_dim(piece, index * count, count, 1)
        return apply_block(total, block, targets, target_box, radius)

    return lax.fori_loop(0, piece.shape[1] // count, one, total)


def per_device(
    centres,
    coeffs,
    residual,
    direction_prev,
    smoothing,
    norm_prev,
    support_radius,
    volume_nodes,
    block_lists,
):
    radius = support_radius[0].astype(jnp.float32) * RADIUS_UNIT
    count = centres.shape[1]
    n_grp = lax.axis_size("grp")
    n_blk = lax.axis_size("blk")
    scaling = 1.0 + smoothing
    precond = residual / scaling

    sector = lax.all_gather(
        jnp.concatenate([centres, coeffs, precond, direction_prev], axis=0), "grp", axis=1, tiled=True
    )

    bundle = jnp.concatenate([centres, precond, direction_prev], axis=0)
    up = [(i, i + 1) for i in range(n_grp - 1)]
    down = [(i + 1, i) for i in range(n_grp - 1)]
    before = lax.ppermute(bundle, "grp", up)
    after = lax.ppermute(bundle, "grp", down)
    widened = jnp.concatenate([before, bundle, after], axis=1)
    arrivals = [lax.ppermute(widened, "blk", xor_pairs(n_blk, mask)) for mask in range(1, n_blk)]

    target_box = box(centres)
    total = jnp.zeros((6, count), jnp.float32)
    total = apply_piece(total, widened, centres, target_box, count, radius)
    total = apply_piece(total, jnp.concatenate(arrivals, axis=1), centres, target_box, count, radius)
    image_p = smoothing * precond + total[:3]
    image_d = smoothing * direction_prev + total[3:]

    node_box = box(volume_nodes)
    listed = block_lists[0]
    def one_entry(slot, evaluation):
        block = lax.dynamic_slice_in_dim(sector, listed[slot] * count, count, 1)
        return apply_block(evaluation, block, volume_nodes, node_box, radius)

    evaluation = lax.fori_loop(
        0, listed.shape[0], one_entry, jnp.zeros((9, volume_nodes.shape[1]), jnp.float32)
    )

    inverse = 1.0 / scaling
    terms = [
        residual * precond,
        precond * image_p,
        precond * image_d + direction_prev * image_p,
        direction_prev * image_d,
        residual * residual * inverse,
        residual * image_p * inverse,
        residual * image_d * inverse,
        image_p * image_p * inverse,
        image_p * image_d * inverse,
        image_d * image_d * inverse,
    ]
    sums = all_sum(jnp.concatenate([jnp.sum(t, axis=1) for t in terms]))
    n0, ca, cb, cc, r0, r1, r2, q0, q1, q2 = (sums[3 * i:3 * i + 3] for i in range(10))
    norm_now = n0
    beta = norm_now / norm_prev
    curvature = ca + beta * (cb + beta * cc)
    alpha = norm_now / curvature
    direction = precond + beta[:, None] * direction_prev
    image = image_p + beta[:, None] * image_d
    coeffs_next = coeffs + alpha[:, None] * direction
    residual_next = residual - alpha[:, None] * image
    norm_next = r0 - 2.0 * alpha * (r1 + beta * r2) + alpha * alpha * (q0 + beta * (2.0 * q1 + beta * q2))
    displacement = evaluation[:3] + alpha[:, None] * (evaluation[3:6] + beta[:, None] * evaluation[6:])
    return (coeffs_next, residual_next, direction, norm_next, displacement)


def solution(mesh):
    placed = (
        P(None, ("blk", "grp")),
        P(None, ("blk", "grp")),
        P(None, ("blk", "grp")),
        P(None, ("blk", "grp")),
        P(("blk", "grp")),
        P(),
        P(),
        P(None, ("blk", "grp")),
        P(("blk", "grp"), None),
    )
    return jax.shard_map(
        per_device,
        mesh=mesh,
        in_specs=placed,
        out_specs=(
            P(None, ("blk", "grp")),
            P(None, ("blk", "grp")),
            P(None, ("blk", "grp")),
            P(),
            P(None, ("blk", "grp")),
        ),
        check_vma=False,
    )
```

```python
import jax
import jax.numpy as jnp
from jax import lax
from jax.sharding import PartitionSpec as P

RADIUS_UNIT = 0.001


def xor_pairs(size, mask):
    return [(i, i ^ mask) for i in range(size)]


def all_sum(value):
    for axis in ("grp", "blk"):
        size = lax.axis_size(axis)
        mask = 1
        while mask < size:
            value = value + lax.ppermute(value, axis, xor_pairs(size, mask))
            mask *= 2
    return value


def wendland(sources, targets, radius):
    apart_first = sources[0][:, None] - targets[0][None, :]
    apart_second = sources[1][:, None] - targets[1][None, :]
    apart_third = sources[2][:, None] - targets[2][None, :]
    distance = jnp.sqrt(
        apart_first * apart_first + apart_second * apart_second + apart_third * apart_third
    )
    scaled = distance / radius
    remain = jnp.maximum(1.0 - scaled, 0.0)
    square = remain * remain
    return square * square * (4.0 * scaled + 1.0)


def apply_block(total, block, targets, radius):
    weights = wendland(block[:3], targets, radius)
    return total + jnp.dot(
        block[3:], weights, preferred_element_type=jnp.float32, precision=lax.Precision.HIGH
    )


def apply_piece(total, piece, targets, count, radius):
    def one(index, total):
        block = lax.dynamic_slice_in_dim(piece, index * count, count, 1)
        return apply_block(total, block, targets, radius)

    return lax.fori_loop(0, piece.shape[1] // count, one, total)


def per_device(
    centres,
    coeffs,
    residual,
    direction_prev,
    smoothing,
    norm_prev,
    support_radius,
    volume_nodes,
    block_lists,
):
    radius = support_radius[0].astype(jnp.float32) * RADIUS_UNIT
    count = centres.shape[1]
    n_grp = lax.axis_size("grp")
    n_blk = lax.axis_size("blk")
    scaling = 1.0 + smoothing
    precond = residual / scaling

    sector = lax.all_gather(
        jnp.concatenate([centres, coeffs, precond, direction_prev], axis=0), "grp", axis=1, tiled=True
    )

    bundle = jnp.concatenate([centres, precond, direction_prev], axis=0)
    up = [(i, i + 1) for i in range(n_grp - 1)]
    down = [(i + 1, i) for i in range(n_grp - 1)]
    before = lax.ppermute(bundle, "grp", up)
    after = lax.ppermute(bundle, "grp", down)
    widened = jnp.concatenate([before, bundle, after], axis=1)
    arrivals = [lax.ppermute(widened, "blk", xor_pairs(n_blk, mask)) for mask in range(1, n_blk)]

    total = jnp.zeros((6, count), jnp.float32)
    total = apply_piece(total, widened, centres, count, radius)
    total = apply_piece(total, jnp.concatenate(arrivals, axis=1), centres, count, radius)
    image_p = smoothing * precond + total[:3]
    image_d = smoothing * direction_prev + total[3:]

    listed = block_lists[0]
    def one_entry(slot, evaluation):
        block = lax.dynamic_slice_in_dim(sector, listed[slot] * count, count, 1)
        return apply_block(evaluation, block, volume_nodes, radius)

    evaluation = lax.fori_loop(
        0, listed.shape[0], one_entry, jnp.zeros((9, volume_nodes.shape[1]), jnp.float32)
    )

    inverse = 1.0 / scaling
    terms = [
        residual * precond,
        precond * image_p,
        precond * image_d + direction_prev * image_p,
        direction_prev * image_d,
        residual * residual * inverse,
        residual * image_p * inverse,
        residual * image_d * inverse,
        image_p * image_p * inverse,
        image_p * image_d * inverse,
        image_d * image_d * inverse,
    ]
    sums = all_sum(jnp.concatenate([jnp.sum(t, axis=1) for t in terms]))
    n0, ca, cb, cc, r0, r1, r2, q0, q1, q2 = (sums[3 * i:3 * i + 3] for i in range(10))
    norm_now = n0
    beta = norm_now / norm_prev
    curvature = ca + beta * (cb + beta * cc)
    alpha = norm_now / curvature
    direction = precond + beta[:, None] * direction_prev
    image = image_p + beta[:, None] * image_d
    coeffs_next = coeffs + alpha[:, None] * direction
    residual_next = residual - alpha[:, None] * image
    norm_next = r0 - 2.0 * alpha * (r1 + beta * r2) + alpha * alpha * (q0 + beta * (2.0 * q1 + beta * q2))
    displacement = evaluation[:3] + alpha[:, None] * (evaluation[3:6] + beta[:, None] * evaluation[6:])
    return (coeffs_next, residual_next, direction, norm_next, displacement)


def solution(mesh):
    placed = (
        P(None, ("blk", "grp")),
        P(None, ("blk", "grp")),
        P(None, ("blk", "grp")),
        P(None, ("blk", "grp")),
        P(("blk", "grp")),
        P(),
        P(),
        P(None, ("blk", "grp")),
        P(("blk", "grp"), None),
    )
    return jax.shard_map(
        per_device,
        mesh=mesh,
        in_specs=placed,
        out_specs=(
            P(None, ("blk", "grp")),
            P(None, ("blk", "grp")),
            P(None, ("blk", "grp")),
            P(),
            P(None, ("blk", "grp")),
        ),
        check_vma=False,
    )
```

```python
import jax
import jax.numpy as jnp
from jax import lax
from jax.sharding import PartitionSpec as P

RADIUS_UNIT = 0.001


def xor_pairs(size, mask):
    return [(i, i ^ mask) for i in range(size)]


def all_sum(value):
    for axis in ("grp", "blk"):
        size = lax.axis_size(axis)
        mask = 1
        while mask < size:
            if mask * 4 <= size:
                first = lax.ppermute(value, axis, xor_pairs(size, mask))
                second = lax.ppermute(value, axis, xor_pairs(size, 2 * mask))
                third = lax.ppermute(value, axis, xor_pairs(size, 3 * mask))
                value = (value + first) + (second + third)
                mask *= 4
            else:
                value = value + lax.ppermute(value, axis, xor_pairs(size, mask))
                mask *= 2
    return value


def wendland(sources, targets, radius):
    apart_first = sources[0][:, None] - targets[0][None, :]
    apart_second = sources[1][:, None] - targets[1][None, :]
    apart_third = sources[2][:, None] - targets[2][None, :]
    distance = jnp.sqrt(
        apart_first * apart_first + apart_second * apart_second + apart_third * apart_third
    )
    scaled = distance / radius
    remain = jnp.maximum(1.0 - scaled, 0.0)
    square = remain * remain
    return square * square * (4.0 * scaled + 1.0)


def apply_block(total, block, targets, radius):
    weights = wendland(block[:3], targets, radius)
    return total + jnp.dot(
        block[3:], weights, preferred_element_type=jnp.float32, precision=lax.Precision.HIGH
    )


def apply_piece(total, piece, targets, count, radius):
    def one(index, total):
        block = lax.dynamic_slice_in_dim(piece, index * count, count, 1)
        return apply_block(total, block, targets, radius)

    return lax.fori_loop(0, piece.shape[1] // count, one, total)


def per_device(
    centres,
    coeffs,
    residual,
    direction_prev,
    smoothing,
    norm_prev,
    support_radius,
    volume_nodes,
    block_lists,
):
    radius = support_radius[0].astype(jnp.float32) * RADIUS_UNIT
    count = centres.shape[1]
    n_grp = lax.axis_size("grp")
    n_blk = lax.axis_size("blk")
    scaling = 1.0 + smoothing
    precond = residual / scaling

    sector = lax.all_gather(
        jnp.concatenate([centres, coeffs, precond, direction_prev], axis=0), "grp", axis=1, tiled=True
    )

    bundle = jnp.concatenate([centres, precond, direction_prev], axis=0)
    up = [(i, i + 1) for i in range(n_grp - 1)]
    down = [(i + 1, i) for i in range(n_grp - 1)]
    before = lax.ppermute(bundle, "grp", up)
    after = lax.ppermute(bundle, "grp", down)
    widened = jnp.concatenate([before, bundle, after], axis=1)
    arrivals = [lax.ppermute(widened, "blk", xor_pairs(n_blk, mask)) for mask in range(1, n_blk)]

    total = jnp.zeros((6, count), jnp.float32)
    total = apply_piece(total, widened, centres, count, radius)
    total = apply_piece(total, jnp.concatenate(arrivals, axis=1), centres, count, radius)
    image_p = smoothing * precond + total[:3]
    image_d = smoothing * direction_prev + total[3:]

    listed = block_lists[0]
    chosen = jnp.concatenate(
        [lax.dynamic_slice_in_dim(sector, listed[slot] * count, count, 1) for slot in range(listed.shape[0])],
        axis=1,
    )
    evaluation = apply_piece(
        jnp.zeros((9, volume_nodes.shape[1]), jnp.float32), chosen, volume_nodes, count, radius
    )

    inverse = 1.0 / scaling
    terms = [
        residual * precond,
        precond * image_p,
        precond * image_d + direction_prev * image_p,
        direction_prev * image_d,
        residual * residual * inverse,
        residual * image_p * inverse,
        residual * image_d * inverse,
        image_p * image_p * inverse,
        image_p * image_d * inverse,
        image_d * image_d * inverse,
    ]
    sums = all_sum(jnp.concatenate([jnp.sum(t, axis=1) for t in terms]))
    n0, ca, cb, cc, r0, r1, r2, q0, q1, q2 = (sums[3 * i:3 * i + 3] for i in range(10))
    norm_now = n0
    beta = norm_now / norm_prev
    curvature = ca + beta * (cb + beta * cc)
    alpha = norm_now / curvature
    direction = precond + beta[:, None] * direction_prev
    image = image_p + beta[:, None] * image_d
    coeffs_next = coeffs + alpha[:, None] * direction
    residual_next = residual - alpha[:, None] * image
    norm_next = r0 - 2.0 * alpha * (r1 + beta * r2) + alpha * alpha * (q0 + beta * (2.0 * q1 + beta * q2))
    displacement = evaluation[:3] + alpha[:, None] * (evaluation[3:6] + beta[:, None] * evaluation[6:])
    return (coeffs_next, residual_next, direction, norm_next, displacement)


def solution(mesh):
    placed = (
        P(None, ("blk", "grp")),
        P(None, ("blk", "grp")),
        P(None, ("blk", "grp")),
        P(None, ("blk", "grp")),
        P(("blk", "grp")),
        P(),
        P(),
        P(None, ("blk", "grp")),
        P(("blk", "grp"), None),
    )
    return jax.shard_map(
        per_device,
        mesh=mesh,
        in_specs=placed,
        out_specs=(
            P(None, ("blk", "grp")),
            P(None, ("blk", "grp")),
            P(None, ("blk", "grp")),
            P(),
            P(None, ("blk", "grp")),
        ),
        check_vma=False,
    )
```

```python
import jax
import jax.numpy as jnp
from jax import lax
from jax.sharding import PartitionSpec as P

RADIUS_UNIT = 0.001


def xor_pairs(size, mask):
    return [(i, i ^ mask) for i in range(size)]


def all_sum(value):
    for axis in ("grp", "blk"):
        size = lax.axis_size(axis)
        mask = 1
        while mask < size:
            if mask * 4 <= size:
                first = lax.ppermute(value, axis, xor_pairs(size, mask))
                second = lax.ppermute(value, axis, xor_pairs(size, 2 * mask))
                third = lax.ppermute(value, axis, xor_pairs(size, 3 * mask))
                value = (value + first) + (second + third)
                mask *= 4
            else:
                value = value + lax.ppermute(value, axis, xor_pairs(size, mask))
                mask *= 2
    return value


def wendland(sources, targets, radius):
    apart_first = sources[0][:, None] - targets[0][None, :]
    apart_second = sources[1][:, None] - targets[1][None, :]
    apart_third = sources[2][:, None] - targets[2][None, :]
    distance = jnp.sqrt(
        apart_first * apart_first + apart_second * apart_second + apart_third * apart_third
    )
    scaled = distance / radius
    remain = jnp.maximum(1.0 - scaled, 0.0)
    square = remain * remain
    return square * square * (4.0 * scaled + 1.0)


def apply_block(total, block, targets, radius):
    weights = wendland(block[:3], targets, radius)
    return total + jnp.dot(
        block[3:], weights, preferred_element_type=jnp.float32, precision=lax.Precision.HIGH
    )


def apply_piece(total, piece, targets, count, radius):
    def one(index, total):
        block = lax.dynamic_slice_in_dim(piece, index * count, count, 1)
        return apply_block(total, block, targets, radius)

    return lax.fori_loop(0, piece.shape[1] // count, one, total)


def per_device(
    centres,
    coeffs,
    residual,
    direction_prev,
    smoothing,
    norm_prev,
    support_radius,
    volume_nodes,
    block_lists,
):
    radius = support_radius[0].astype(jnp.float32) * RADIUS_UNIT
    count = centres.shape[1]
    n_grp = lax.axis_size("grp")
    n_blk = lax.axis_size("blk")
    scaling = 1.0 + smoothing
    precond = residual / scaling

    sector = lax.all_gather(
        jnp.concatenate([centres, coeffs, precond, direction_prev], axis=0), "grp", axis=1, tiled=True
    )

    bundle = jnp.concatenate([centres, precond, direction_prev], axis=0)
    up = [(i, i + 1) for i in range(n_grp - 1)]
    down = [(i + 1, i) for i in range(n_grp - 1)]
    before = lax.ppermute(bundle, "grp", up)
    after = lax.ppermute(bundle, "grp", down)
    widened = jnp.concatenate([before, bundle, after], axis=1)
    arrivals = [lax.ppermute(widened, "blk", xor_pairs(n_blk, mask)) for mask in range(1, n_blk)]

    total = jnp.zeros((6, count), jnp.float32)
    total = apply_piece(total, jnp.concatenate([widened] + arrivals, axis=1), centres, count, radius)
    image_p = smoothing * precond + total[:3]
    image_d = smoothing * direction_prev + total[3:]

    listed = block_lists[0]
    chosen = jnp.concatenate(
        [lax.dynamic_slice_in_dim(sector, listed[slot] * count, count, 1) for slot in range(listed.shape[0])],
        axis=1,
    )
    evaluation = apply_piece(
        jnp.zeros((9, volume_nodes.shape[1]), jnp.float32), chosen, volume_nodes, count, radius
    )

    inverse = 1.0 / scaling
    terms = [
        residual * precond,
        precond * image_p,
        precond * image_d + direction_prev * image_p,
        direction_prev * image_d,
        residual * residual * inverse,
        residual * image_p * inverse,
        residual * image_d * inverse,
        image_p * image_p * inverse,
        image_p * image_d * inverse,
        image_d * image_d * inverse,
    ]
    sums = all_sum(jnp.concatenate([jnp.sum(t, axis=1) for t in terms]))
    n0, ca, cb, cc, r0, r1, r2, q0, q1, q2 = (sums[3 * i:3 * i + 3] for i in range(10))
    norm_now = n0
    beta = norm_now / norm_prev
    curvature = ca + beta * (cb + beta * cc)
    alpha = norm_now / curvature
    direction = precond + beta[:, None] * direction_prev
    image = image_p + beta[:, None] * image_d
    coeffs_next = coeffs + alpha[:, None] * direction
    residual_next = residual - alpha[:, None] * image
    norm_next = r0 - 2.0 * alpha * (r1 + beta * r2) + alpha * alpha * (q0 + beta * (2.0 * q1 + beta * q2))
    displacement = evaluation[:3] + alpha[:, None] * (evaluation[3:6] + beta[:, None] * evaluation[6:])
    return (coeffs_next, residual_next, direction, norm_next, displacement)


def solution(mesh):
    placed = (
        P(None, ("blk", "grp")),
        P(None, ("blk", "grp")),
        P(None, ("blk", "grp")),
        P(None, ("blk", "grp")),
        P(("blk", "grp")),
        P(),
        P(),
        P(None, ("blk", "grp")),
        P(("blk", "grp"), None),
    )
    return jax.shard_map(
        per_device,
        mesh=mesh,
        in_specs=placed,
        out_specs=(
            P(None, ("blk", "grp")),
            P(None, ("blk", "grp")),
            P(None, ("blk", "grp")),
            P(),
            P(None, ("blk", "grp")),
        ),
        check_vma=False,
    )
```

```python
import jax
import jax.numpy as jnp
from jax import lax
from jax.sharding import PartitionSpec as P

RADIUS_UNIT = 0.001


def xor_pairs(size, mask):
    return [(i, i ^ mask) for i in range(size)]


def all_sum(value):
    for axis in ("grp", "blk"):
        size = lax.axis_size(axis)
        mask = 1
        while mask < size:
            if mask * 4 <= size:
                first = lax.ppermute(value, axis, xor_pairs(size, mask))
                second = lax.ppermute(value, axis, xor_pairs(size, 2 * mask))
                third = lax.ppermute(value, axis, xor_pairs(size, 3 * mask))
                value = (value + first) + (second + third)
                mask *= 4
            else:
                value = value + lax.ppermute(value, axis, xor_pairs(size, mask))
                mask *= 2
    return value


def wendland(sources, targets, radius):
    apart_first = sources[0][:, None] - targets[0][None, :]
    apart_second = sources[1][:, None] - targets[1][None, :]
    apart_third = sources[2][:, None] - targets[2][None, :]
    distance = jnp.sqrt(
        apart_first * apart_first + apart_second * apart_second + apart_third * apart_third
    )
    scaled = distance * (1.0 / radius)
    remain = jnp.maximum(1.0 - scaled, 0.0)
    square = remain * remain
    return square * square * (4.0 * scaled + 1.0)


def apply_block(total, block, targets, radius):
    weights = wendland(block[:3], targets, radius)
    return total + jnp.dot(
        block[3:], weights, preferred_element_type=jnp.float32, precision=lax.Precision.HIGH
    )


def apply_piece(total, piece, targets, count, radius):
    def one(index, total):
        block = lax.dynamic_slice_in_dim(piece, index * count, count, 1)
        return apply_block(total, block, targets, radius)

    return lax.fori_loop(0, piece.shape[1] // count, one, total)


def per_device(
    centres,
    coeffs,
    residual,
    direction_prev,
    smoothing,
    norm_prev,
    support_radius,
    volume_nodes,
    block_lists,
):
    radius = support_radius[0].astype(jnp.float32) * RADIUS_UNIT
    count = centres.shape[1]
    n_grp = lax.axis_size("grp")
    n_blk = lax.axis_size("blk")
    scaling = 1.0 + smoothing
    precond = residual / scaling

    sector = lax.all_gather(
        jnp.concatenate([centres, coeffs, precond, direction_prev], axis=0), "grp", axis=1, tiled=True
    )

    bundle = jnp.concatenate([centres, precond, direction_prev], axis=0)
    up = [(i, i + 1) for i in range(n_grp - 1)]
    down = [(i + 1, i) for i in range(n_grp - 1)]
    before = lax.ppermute(bundle, "grp", up)
    after = lax.ppermute(bundle, "grp", down)
    widened = jnp.concatenate([before, bundle, after], axis=1)
    arrivals = [lax.ppermute(widened, "blk", xor_pairs(n_blk, mask)) for mask in range(1, n_blk)]

    total = jnp.zeros((6, count), jnp.float32)
    total = apply_piece(total, widened, centres, count, radius)
    total = apply_piece(total, jnp.concatenate(arrivals, axis=1), centres, count, radius)
    image_p = smoothing * precond + total[:3]
    image_d = smoothing * direction_prev + total[3:]

    listed = block_lists[0]
    chosen = jnp.concatenate(
        [lax.dynamic_slice_in_dim(sector, listed[slot] * count, count, 1) for slot in range(listed.shape[0])],
        axis=1,
    )
    evaluation = apply_piece(
        jnp.zeros((9, volume_nodes.shape[1]), jnp.float32), chosen, volume_nodes, count, radius
    )

    inverse = 1.0 / scaling
    terms = [
        residual * precond,
        precond * image_p,
        precond * image_d + direction_prev * image_p,
        direction_prev * image_d,
        residual * residual * inverse,
        residual * image_p * inverse,
        residual * image_d * inverse,
        image_p * image_p * inverse,
        image_p * image_d * inverse,
        image_d * image_d * inverse,
    ]
    sums = all_sum(jnp.concatenate([jnp.sum(t, axis=1) for t in terms]))
    n0, ca, cb, cc, r0, r1, r2, q0, q1, q2 = (sums[3 * i:3 * i + 3] for i in range(10))
    norm_now = n0
    beta = norm_now / norm_prev
    curvature = ca + beta * (cb + beta * cc)
    alpha = norm_now / curvature
    direction = precond + beta[:, None] * direction_prev
    image = image_p + beta[:, None] * image_d
    coeffs_next = coeffs + alpha[:, None] * direction
    residual_next = residual - alpha[:, None] * image
    norm_next = r0 - 2.0 * alpha * (r1 + beta * r2) + alpha * alpha * (q0 + beta * (2.0 * q1 + beta * q2))
    displacement = evaluation[:3] + alpha[:, None] * (evaluation[3:6] + beta[:, None] * evaluation[6:])
    return (coeffs_next, residual_next, direction, norm_next, displacement)


def solution(mesh):
    placed = (
        P(None, ("blk", "grp")),
        P(None, ("blk", "grp")),
        P(None, ("blk", "grp")),
        P(None, ("blk", "grp")),
        P(("blk", "grp")),
        P(),
        P(),
        P(None, ("blk", "grp")),
        P(("blk", "grp"), None),
    )
    return jax.shard_map(
        per_device,
        mesh=mesh,
        in_specs=placed,
        out_specs=(
            P(None, ("blk", "grp")),
            P(None, ("blk", "grp")),
            P(None, ("blk", "grp")),
            P(),
            P(None, ("blk", "grp")),
        ),
        check_vma=False,
    )
```

```python
import jax
import jax.numpy as jnp
from jax import lax
from jax.sharding import PartitionSpec as P


RADIUS_UNIT = 0.001


def xor_pairs(size, mask):
    return [(i, i ^ mask) for i in range(size)]


def all_sum(value):
    for axis in ("grp", "blk"):
        size = lax.axis_size(axis)
        mask = 1
        while mask < size:
            if mask * 4 <= size:
                first = lax.ppermute(value, axis, xor_pairs(size, mask))
                second = lax.ppermute(value, axis, xor_pairs(size, 2 * mask))
                third = lax.ppermute(value, axis, xor_pairs(size, 3 * mask))
                value = (value + first) + (second + third)
                mask *= 4
            else:
                value = value + lax.ppermute(value, axis, xor_pairs(size, mask))
                mask *= 2
    return value


def wendland(sources, targets, radius):
    apart_first = sources[0][:, None] - targets[0][None, :]
    apart_second = sources[1][:, None] - targets[1][None, :]
    apart_third = sources[2][:, None] - targets[2][None, :]
    distance = jnp.sqrt(
        apart_first * apart_first + apart_second * apart_second + apart_third * apart_third
    )
    scaled = distance * (1.0 / radius)
    remain = jnp.maximum(1.0 - scaled, 0.0)
    square = remain * remain
    return square * square * (4.0 * scaled + 1.0)


def apply_block(total, block, targets, radius):
    weights = wendland(block[:3], targets, radius)
    return total + jnp.dot(
        block[3:], weights, preferred_element_type=jnp.float32, precision=lax.Precision.HIGH
    )


def apply_piece(total, piece, targets, count, radius):
    def one(index, total):
        block = lax.dynamic_slice_in_dim(piece, index * count, count, 1)
        return apply_block(total, block, targets, radius)

    return lax.fori_loop(0, piece.shape[1] // count, one, total)


def per_device(
    centres,
    coeffs,
    residual,
    direction_prev,
    smoothing,
    norm_prev,
    support_radius,
    volume_nodes,
    block_lists,
):
    radius = support_radius[0].astype(jnp.float32) * RADIUS_UNIT
    count = centres.shape[1]
    n_grp = lax.axis_size("grp")
    n_blk = lax.axis_size("blk")
    scaling = 1.0 + smoothing
    precond = residual / scaling

    sector = lax.all_gather(
        jnp.concatenate([centres, coeffs, precond, direction_prev], axis=0), "grp", axis=1, tiled=True
    )

    bundle = jnp.concatenate([centres, precond, direction_prev], axis=0)
    up = [(i, i + 1) for i in range(n_grp - 1)]
    down = [(i + 1, i) for i in range(n_grp - 1)]
    before = lax.ppermute(bundle, "grp", up)
    after = lax.ppermute(bundle, "grp", down)
    widened = jnp.concatenate([before, bundle, after], axis=1)
    arrivals = [lax.ppermute(widened, "blk", xor_pairs(n_blk, mask)) for mask in range(1, n_blk)]

    total = jnp.zeros((6, count), jnp.float32)
    total = apply_piece(total, widened, centres, count, radius)
    total = apply_piece(total, jnp.concatenate(arrivals, axis=1), centres, count, radius)
    image_p = smoothing * precond + total[:3]
    image_d = smoothing * direction_prev + total[3:]

    listed = block_lists[0]
    chosen = jnp.concatenate(
        [lax.dynamic_slice_in_dim(sector, listed[slot] * count, count, 1) for slot in range(listed.shape[0])],
        axis=1,
    )
    halves = []
    half = chosen.shape[1] // 2
    for part in range(2):
        halves.append(
            apply_piece(
                jnp.zeros((9, volume_nodes.shape[1]), jnp.float32),
                chosen[:, part * half:(part + 1) * half],
                volume_nodes,
                count,
                radius,
            )
        )
    evaluation = halves[0] + halves[1]

    inverse = 1.0 / scaling
    terms = [
        residual * precond,
        precond * image_p,
        precond * image_d + direction_prev * image_p,
        direction_prev * image_d,
        residual * residual * inverse,
        residual * image_p * inverse,
        residual * image_d * inverse,
        image_p * image_p * inverse,
        image_p * image_d * inverse,
        image_d * image_d * inverse,
    ]
    sums = all_sum(jnp.concatenate([jnp.sum(t, axis=1) for t in terms]))
    n0, ca, cb, cc, r0, r1, r2, q0, q1, q2 = (sums[3 * i:3 * i + 3] for i in range(10))
    norm_now = n0
    beta = norm_now / norm_prev
    curvature = ca + beta * (cb + beta * cc)
    alpha = norm_now / curvature
    direction = precond + beta[:, None] * direction_prev
    image = image_p + beta[:, None] * image_d
    coeffs_next = coeffs + alpha[:, None] * direction
    residual_next = residual - alpha[:, None] * image
    norm_next = r0 - 2.0 * alpha * (r1 + beta * r2) + alpha * alpha * (q0 + beta * (2.0 * q1 + beta * q2))
    displacement = evaluation[:3] + alpha[:, None] * (evaluation[3:6] + beta[:, None] * evaluation[6:])
    return (coeffs_next, residual_next, direction, norm_next, displacement)


def solution(mesh):
    placed = (
        P(None, ("blk", "grp")),
        P(None, ("blk", "grp")),
        P(None, ("blk", "grp")),
        P(None, ("blk", "grp")),
        P(("blk", "grp")),
        P(),
        P(),
        P(None, ("blk", "grp")),
        P(("blk", "grp"), None),
    )
    return jax.shard_map(
        per_device,
        mesh=mesh,
        in_specs=placed,
        out_specs=(
            P(None, ("blk", "grp")),
            P(None, ("blk", "grp")),
            P(None, ("blk", "grp")),
            P(),
            P(None, ("blk", "grp")),
        ),
        check_vma=False,
    )
```
